256 devices in a mesh: dp: 4 (over x), expert: 64 (over z, y, core).
Axes of the slice: x: 4, y: 4, z: 8, core: 2. Of those that a mesh axis runs over, the one named last changes fastest.
Arguments:
- tokens: bfloat16 [4096, 2048], P(('dp', 'expert')), may hold values from -6 to 6
- expert_ids: int32 [4096, 8], P(('dp', 'expert')), may hold values from 0 to 127, all different within a row; in each aligned block of 16 rows (0 to 15, 16 to 31, ...) at most 2 rows name the same one
- gate_weights: float32 [4096, 8], P(('dp', 'expert')), may hold values from 0.1 to 1
- hot_experts: int32 [2], replicated, may hold values from 0 to 127, as said below
- capacity: int32 [128], replicated, may hold values from 32 to 64
- w_in: bfloat16 [128, 2048, 1536], P('expert', None, 'dp'), may hold values from -0.125 to 0.125
- w_out: bfloat16 [128, 1536, 2048], P('expert', 'dp'), may hold values from -0.15625 to 0.15625
- grad_y: bfloat16 [4096, 2048], P(('dp', 'expert')), may hold values from -1.5 to 1.5
Outputs:
- mixed: bfloat16 [4096, 2048], P(('dp', 'expert'))
- token_grad: bfloat16 [4096, 2048], P(('dp', 'expert'))
- gate_grad: float32 [4096, 8], P(('dp', 'expert'))
- grad_w_in: bfloat16 [128, 2048, 1536], P('expert', None, 'dp')
- grad_w_out: bfloat16 [128, 1536, 2048], P('expert', 'dp')
The draws below stay inside these ranges and needn't reach their ends.
Inputs may be any that keep to these rules, and one draw needn't show every extreme that they name: `expert_ids`: among the tokens of one device no expert is named more than 2 times, a bound that some block reaches. `hot_experts`: 2 different experts; the last entry is always expert 128 - 1.
All inputs are finite; a program needn't handle non-finite values.
Results may differ from the reference program's by a relative error of at most 0.012.
Values may be sent and summed in bfloat16 or wider, within the bound.
No kernel may reach another device: no remote copies, remote signals or barrier semaphores. Data moves between devices by JAX's collectives and lax.ppermute only.
A program may use at most 128 MiB of HBM per device.

```python
import math
import jax
import jax.numpy as jnp
import numpy as np
from jax import lax

D = 2048
H = 1536
TOP = 8
HOT = 2
TOK_DEV = 16
EXPERTS = 128
SLOT = 2
CAP = 64
TOKENS = 4096
N_DP = 4
N_EXPERT = 64


def draw_hot_experts(key, part):
    others = jax.random.permutation(key, EXPERTS - 1)[:HOT - 1].astype(jnp.int32)
    return jnp.concatenate([others, jnp.full((1,), EXPERTS - 1, jnp.int32)])


def draw_capacity(key, part):
    first_key, second_key = jax.random.split(key)
    values = jax.random.randint(first_key, (EXPERTS,), CAP // 2, CAP + 1, dtype=jnp.int32)
    spot_idx = jax.random.randint(second_key, (), 0, EXPERTS, dtype=jnp.int32)
    return values.at[spot_idx].set(CAP)


def steps_of(stream_key, extent, cuts, least, top_value):
    loudness = 1.0
    for dim, shards_of in cuts:
        draws = jax.random.uniform(jax.random.fold_in(jax.random.fold_in(stream_key, 6), dim), (shards_of,), jnp.float32, least / len(cuts), top_value / len(cuts))
        loudness = loudness * jnp.repeat(jnp.exp(draws), extent[dim] // shards_of).reshape((-1,) + (1,) * (len(extent) - 1 - dim))
    return loudness


def assign_block(own_key, own, number, rows, number_of, top, bound, slope):
    ranking = jax.random.permutation(own_key, number_of)
    crowded, usual = shares(number_of, rows * top, bound, slope, True), shares(number_of, rows * top, bound, slope, False)
    places = jnp.arange(number_of)

    def named(lengths, turn):
        used = int((lengths > 0).sum())
        fixed = max(1, used // 4)
        passed = fixed + (places - fixed + turn * (used - fixed)) % max(1, number_of - fixed)
        return jnp.zeros((number_of,), jnp.int32).at[ranking[jnp.where(places < fixed, places, passed)]].set(jnp.asarray(lengths, jnp.int32))

    lengths = jnp.where(number % 4 == 0, named(crowded, number // 4), named(usual, number - number // 4 - 1))
    mixed = jax.random.permutation(jax.random.fold_in(own, 3), number_of)
    giver, receiver = mixed[0:number_of // 2 * 2:2], mixed[1:number_of // 2 * 2:2]
    margin = jnp.minimum(lengths[giver] - 1, bound - lengths[receiver]) // 2
    margin = jnp.where((giver == ranking[0]) | (receiver == ranking[0]) | (lengths[receiver] == 0), 0, jnp.maximum(margin, 0))
    passed = jax.random.randint(jax.random.fold_in(own, 4), (number_of // 2,), 0, 1 << 20) % (margin + 1)
    lengths = lengths.at[giver].add(-passed).at[receiver].add(passed)
    items = jnp.searchsorted(jnp.cumsum(lengths), jnp.arange(rows * top), side="right").astype(jnp.int32)
    table = items.reshape(top, rows).T
    table = table[jax.random.permutation(jax.random.fold_in(own, 1), rows)]
    turn = jax.random.randint(jax.random.fold_in(own, 2), (rows, 1), 0, top)
    return jnp.take_along_axis(table, (jnp.arange(top)[None, :] + turn) % top, axis=1)


def shares(count, total, reach, slope, full):
    weights = [(1 << 20) // math.isqrt(rank ** slope) + 1 for rank in range(1, count + 1)]
    largest = reach if full else min(reach, max(-(-total // count), total * weights[0] // sum(weights)))
    least = 1 if total - largest >= count - 1 else 0
    counts, spare = [largest] + [least] * (count - 1), total - largest - least * (count - 1)
    while spare > 0:
        free = [i for i in range(1, count) if counts[i] < largest] or [i for i in range(1, count) if counts[i] < reach]
        mass, budget = sum([weights[i] for i in free]), spare
        for i in free:
            addition = min(reach - counts[i], max(1, budget * weights[i] // mass), spare)
            counts[i] = counts[i] + addition
            spare = spare - addition
    return np.array(counts)


def centred(key, extent, deviation, most, cuts=(), kind=jnp.bfloat16):
    values = jax.random.normal(key, extent, jnp.float32) * deviation
    if len(cuts) > 0:
        values = steps_of(key, extent, cuts, -0.22, 0.18) * values
    return jnp.clip(values, min=-most, max=most).astype(kind)


def setup_inputs(seed: int = 0) -> dict:
    key_list = jax.random.split(jax.random.key(seed), 9)
    tokens = centred(key_list[0], (TOKENS, D), 1.0, 6.0, ((0, 256),))
    expert_ids_keys = jax.random.split(jax.random.fold_in(key_list[1], 1), TOKENS // TOK_DEV)
    expert_ids_turns = jax.random.permutation(jax.random.fold_in(key_list[1], 3), TOKENS // TOK_DEV)
    expert_ids = jax.vmap(lambda own, number: assign_block(jax.random.fold_in(key_list[1], 2), own, number, TOK_DEV, EXPERTS, TOP, SLOT, 2))(expert_ids_keys, expert_ids_turns).reshape((TOKENS, TOP))
    gate_weights = jnp.clip(0.1 + 0.9 * jax.random.uniform(key_list[2], (TOKENS, TOP), jnp.float32) ** steps_of(key_list[2], (TOKENS, TOP), ((0, 256),), -0.2, 0.2), 0.1, 1.0)
    hot_experts = draw_hot_experts(jax.random.fold_in(key_list[8], 71), 0)
    capacity = draw_capacity(jax.random.fold_in(key_list[8], 71), 0)
    w_in = centred(key_list[5], (EXPERTS, D, H), D ** -0.5, 0.125, ((0, 64), (2, 4)))
    w_out = centred(key_list[6], (EXPERTS, H, D), H ** -0.5, 0.15625, ((0, 64), (1, 4)))
    grad_y = centred(key_list[7], (TOKENS, D), 0.25, 1.5, ((0, 256),))
    return dict(tokens=tokens, expert_ids=expert_ids, gate_weights=gate_weights, hot_experts=hot_experts, capacity=capacity, w_in=w_in, w_out=w_out, grad_y=grad_y)


def silu_terms(pre_act):
    sig_val = jax.nn.sigmoid(pre_act)
    return pre_act * sig_val, sig_val * (1.0 + pre_act * (1.0 - sig_val))


def round_keep(values):
    return lax.optimization_barrier(values.astype(jnp.bfloat16)).astype(jnp.float32)


def reference(tokens, expert_ids, gate_weights, hot_experts, capacity, w_in, w_out, grad_y):
    hidden_block = H // N_DP
    group_len = N_EXPERT * TOK_DEV
    labels = jnp.arange(EXPERTS, dtype=jnp.int32)
    per_token = jnp.any(expert_ids[:, :, None] == labels, axis=1).astype(jnp.int32)
    grouped = per_token.reshape(N_DP, group_len, EXPERTS)
    prior = (jnp.cumsum(grouped, axis=1) - grouped).reshape(TOKENS, EXPERTS)
    rank_of = jnp.take_along_axis(prior, expert_ids, axis=1)
    hot_hit = jnp.any(expert_ids[:, :, None] == hot_experts[None, None, :], axis=-1)
    kept = jnp.logical_or(hot_hit, rank_of < capacity[expert_ids])
    assign_count = TOKENS * TOP
    flat_expert = expert_ids.reshape(-1).astype(jnp.int32)
    flat_kept = kept.reshape(-1)
    sort_key = jnp.where(flat_kept, flat_expert, EXPERTS).astype(jnp.int32)
    order_idx = jnp.argsort(sort_key, stable=True).astype(jnp.int32)
    per_expert = jnp.sum((sort_key[:, None] == labels[None, :]).astype(jnp.int32), axis=0)
    starts = (jnp.cumsum(per_expert) - per_expert).astype(jnp.int32)
    window = N_DP * N_EXPERT * SLOT
    order_pad = jnp.concatenate([order_idx, jnp.zeros((window,), jnp.int32)])
    flat_gate = gate_weights.reshape(-1)

    def one_expert(expert):
        idx = lax.dynamic_slice(order_pad, (starts[expert].astype(jnp.int32),), (window,))
        valid = jnp.arange(window, dtype=jnp.int32) < per_expert[expert]
        tok_idx = idx // TOP
        rows_x = jnp.where(valid[:, None], tokens[tok_idx], jnp.zeros((), jnp.bfloat16))
        gate_rows = jnp.where(valid, flat_gate[idx], jnp.float32(0.0))
        rows_g = (gate_rows[:, None] * grad_y[tok_idx].astype(jnp.float32)).astype(jnp.bfloat16)
        weight_in = w_in[expert]
        weight_out = w_out[expert]
        pre_act = jnp.dot(rows_x, weight_in, preferred_element_type=jnp.float32)
        act_full, slope_val = silu_terms(pre_act)
        act_low = act_full.astype(jnp.bfloat16)
        out_parts = jnp.einsum("wgh,ghd->wgd", act_low.astype(jnp.float32).reshape(window, N_DP, hidden_block),
                               weight_out.astype(jnp.float32).reshape(N_DP, hidden_block, D))
        expert_out = jnp.sum(round_keep(out_parts), axis=1).astype(jnp.bfloat16)
        back_act = jnp.dot(rows_g, weight_out.T, preferred_element_type=jnp.float32)
        pre_grad = (back_act * slope_val).astype(jnp.bfloat16)
        in_parts = jnp.einsum("wgh,dgh->wgd", pre_grad.astype(jnp.float32).reshape(window, N_DP, hidden_block),
                              weight_in.astype(jnp.float32).reshape(D, N_DP, hidden_block))
        in_rows = jnp.sum(round_keep(in_parts), axis=1).astype(jnp.bfloat16)
        grad_in = jnp.dot(rows_x.T, pre_grad, preferred_element_type=jnp.float32).astype(jnp.bfloat16)
        grad_out = jnp.dot(act_low.T, rows_g, preferred_element_type=jnp.float32).astype(jnp.bfloat16)
        return expert_out, in_rows, grad_in, grad_out

    out_all, in_all, grad_w_in, grad_w_out = lax.map(one_expert, labels)
    inverse = jnp.zeros((assign_count,), jnp.int32).at[order_idx].set(jnp.arange(assign_count, dtype=jnp.int32))
    position = jnp.clip(inverse - starts[flat_expert], 0, window - 1)
    out_asg = out_all[flat_expert, position].astype(jnp.float32)
    in_asg = in_all[flat_expert, position].astype(jnp.float32)
    keep_f = flat_kept.astype(jnp.float32)[:, None]
    out_asg = (out_asg * keep_f).reshape(TOKENS, TOP, D)
    in_asg = (in_asg * keep_f).reshape(TOKENS, TOP, D)
    mixed = jnp.sum(gate_weights[:, :, None] * out_asg, axis=1).astype(jnp.bfloat16)
    token_grad = jnp.sum(in_asg, axis=1).astype(jnp.bfloat16)
    gate_grad = jnp.sum(grad_y.astype(jnp.float32)[:, None, :] * out_asg, axis=-1)
    return mixed, token_grad, gate_grad, grad_w_in, grad_w_out
```

```python
import jax
import jax.numpy as jnp
from jax import lax
from jax.sharding import PartitionSpec as P


FLAG_COLS = 128


def silu_terms(pre_act):
    sig_val = jax.nn.sigmoid(pre_act)
    return (pre_act * sig_val, sig_val * (1.0 + pre_act * (1.0 - sig_val)))


def expert_math(rows_x, rows_g, weight_in, weight_out):
    pre_act = jnp.einsum("gerd,edh->gerh", rows_x, weight_in, preferred_element_type=jnp.float32)
    act_full, slope_val = silu_terms(pre_act)
    act_low = act_full.astype(jnp.bfloat16)
    out_part = jnp.einsum("gerh,ehd->gerd", act_low, weight_out, preferred_element_type=jnp.float32)
    back_act = jnp.einsum("gerd,ehd->gerh", rows_g, weight_out, preferred_element_type=jnp.float32)
    pre_grad = (back_act * slope_val).astype(jnp.bfloat16)
    in_part = jnp.einsum("gerh,edh->gerd", pre_grad, weight_in, preferred_element_type=jnp.float32)
    grad_in = jnp.einsum("gerd,gerh->edh", rows_x, pre_grad, preferred_element_type=jnp.float32)
    grad_out = jnp.einsum("gerh,gerd->ehd", act_low, rows_g, preferred_element_type=jnp.float32)
    stacked = jnp.stack([out_part, in_part], axis=1)
    return (stacked.astype(jnp.bfloat16), grad_in, grad_out)


def local(tokens, expert_ids, gate_weights, hot_experts, capacity, w_in, w_out, grad_y):
    highest = lax.Precision.HIGHEST
    expert_devs = lax.axis_size("expert")
    tok_rows, top_k = expert_ids.shape
    local_experts = w_in.shape[0]
    expert_total = local_experts * expert_devs
    slot_count = max(2, 3 * tok_rows * top_k // (2 * expert_total))
    feature_dim = tokens.shape[1]
    labels = jnp.arange(expert_total, dtype=jnp.int32)
    name_hit = (expert_ids[:, :, None] == labels).astype(jnp.int32)
    per_token = jnp.sum(name_hit, axis=1)
    within_dev = jnp.cumsum(per_token, axis=0) - per_token
    slot_hit = (within_dev[:, :, None] == jnp.arange(slot_count, dtype=jnp.int32)).astype(
        jnp.float32
    )
    send_picks = name_hit.astype(jnp.float32)[:, :, :, None] * slot_hit[:, None, :, :]
    rows_sel = jnp.sum(send_picks, axis=1)
    gate_sel = jnp.einsum("tkes,tk->tes", send_picks, gate_weights, precision=highest)
    grad_f32 = grad_y.astype(jnp.float32)
    x_buf = jnp.einsum(
        "tes,td->esd", rows_sel.astype(jnp.bfloat16), tokens, preferred_element_type=jnp.float32
    ).astype(jnp.bfloat16)
    g_buf = jnp.einsum("tes,td->esd", gate_sel, grad_f32, precision=highest).astype(jnp.bfloat16)
    flag = jnp.sum(gate_sel, axis=0)
    flag_cols = (jnp.arange(FLAG_COLS) == 0).astype(jnp.float32)
    flag_buf = (flag[:, :, None] * flag_cols).astype(jnp.bfloat16)
    send = jnp.concatenate([x_buf, g_buf, flag_buf], axis=-1)
    send = send.reshape(expert_devs, local_experts, slot_count, 2 * feature_dim + FLAG_COLS)
    recv = lax.all_to_all(send, "expert", split_axis=0, concat_axis=2, tiled=True)[0]
    valid = (recv[:, :, 2 * feature_dim] > 0).astype(jnp.int32)
    rank_of = jnp.cumsum(valid, axis=1) - valid
    mine = lax.axis_index("expert") * local_experts + jnp.arange(local_experts, dtype=jnp.int32)
    is_hot = jnp.any(mine[:, None] == hot_experts[None, :], axis=1)
    keep = (valid > 0) & (is_hot[:, None] | (rank_of < capacity[mine][:, None]))
    rows = jnp.where(keep[:, :, None], recv[:, :, : 2 * feature_dim], jnp.zeros((), jnp.bfloat16))
    rows_all = lax.all_gather(rows, "dp", axis=0, tiled=False)
    xg_all = rows_all[..., :feature_dim]
    gg_all = rows_all[..., feature_dim:]
    partial_terms, grad_wi, grad_wo = expert_math(xg_all, gg_all, w_in, w_out)
    parts = lax.all_to_all(partial_terms, "dp", split_axis=0, concat_axis=0, tiled=True)
    summed = jnp.sum(parts.astype(jnp.float32), axis=0).astype(jnp.bfloat16)
    summed = summed.reshape(2, local_experts, expert_devs, slot_count, feature_dim)
    back = lax.all_to_all(summed, "expert", split_axis=2, concat_axis=2, tiled=True)
    back = jnp.transpose(back, (0, 2, 1, 3, 4)).reshape(2, expert_total, slot_count, feature_dim)
    out_f32 = back[0].astype(jnp.float32)
    in_f32 = back[1].astype(jnp.float32)
    mixed = jnp.einsum("tes,esd->td", gate_sel, out_f32, precision=highest)
    token_grad = jnp.einsum("tes,esd->td", rows_sel, in_f32, precision=highest)
    dot_vals = jnp.einsum("td,esd->tes", grad_f32, out_f32, precision=highest)
    gate_grad = jnp.einsum("tkes,tes->tk", send_picks, dot_vals, precision=highest)
    return (
        mixed.astype(jnp.bfloat16),
        token_grad.astype(jnp.bfloat16),
        gate_grad,
        grad_wi.astype(jnp.bfloat16),
        grad_wo.astype(jnp.bfloat16),
    )


def solution(mesh):
    in_specs = (
        P(("dp", "expert"), None),
        P(("dp", "expert"), None),
        P(("dp", "expert"), None),
        P(),
        P(),
        P("expert", None, "dp"),
        P("expert", "dp", None),
        P(("dp", "expert"), None),
    )
    out_specs = (
        P(("dp", "expert"), None),
        P(("dp", "expert"), None),
        P(("dp", "expert"), None),
        P("expert", None, "dp"),
        P("expert", "dp", None),
    )
    return jax.shard_map(local, mesh=mesh, in_specs=in_specs, out_specs=out_specs, check_vma=False)
```

```python
import jax
import jax.numpy as jnp
from jax import lax
from jax.sharding import PartitionSpec as P


FLAG_COLS = 128


def silu_terms(pre_act):
    sig_val = jax.nn.sigmoid(pre_act)
    return (pre_act * sig_val, sig_val * (1.0 + pre_act * (1.0 - sig_val)))


def expert_math(rows_x, rows_g, weight_in, weight_out):
    pre_act = jnp.einsum("gerd,edh->gerh", rows_x, weight_in, preferred_element_type=jnp.float32)
    act_full, slope_val = silu_terms(pre_act)
    act_low = act_full.astype(jnp.bfloat16)
    out_part = jnp.einsum("gerh,ehd->gerd", act_low, weight_out, preferred_element_type=jnp.float32)
    back_act = jnp.einsum("gerd,ehd->gerh", rows_g, weight_out, preferred_element_type=jnp.float32)
    pre_grad = (back_act * slope_val).astype(jnp.bfloat16)
    in_part = jnp.einsum("gerh,edh->gerd", pre_grad, weight_in, preferred_element_type=jnp.float32)
    grad_in = jnp.einsum("gerd,gerh->edh", rows_x, pre_grad, preferred_element_type=jnp.float32)
    grad_out = jnp.einsum("gerh,gerd->ehd", act_low, rows_g, preferred_element_type=jnp.float32)
    stacked = jnp.stack([out_part, in_part], axis=1)
    return (stacked.astype(jnp.bfloat16), grad_in, grad_out)


def local(tokens, expert_ids, gate_weights, hot_experts, capacity, w_in, w_out, grad_y):
    highest = lax.Precision.HIGHEST
    expert_devs = lax.axis_size("expert")
    tok_rows, top_k = expert_ids.shape
    local_experts = w_in.shape[0]
    expert_total = local_experts * expert_devs
    slot_count = max(2, 3 * tok_rows * top_k // (2 * expert_total))
    feature_dim = tokens.shape[1]
    labels = jnp.arange(expert_total, dtype=jnp.int32)
    name_hit = (expert_ids[:, :, None] == labels).astype(jnp.int32)
    per_token = jnp.sum(name_hit, axis=1)
    within_dev = jnp.cumsum(per_token, axis=0) - per_token
    slot_hit = (within_dev[:, :, None] == jnp.arange(slot_count, dtype=jnp.int32)).astype(
        jnp.float32
    )
    send_picks = name_hit.astype(jnp.float32)[:, :, :, None] * slot_hit[:, None, :, :]
    rows_sel = jnp.sum(send_picks, axis=1)
    gate_sel = jnp.einsum("tkes,tk->tes", send_picks, gate_weights, precision=highest)
    grad_f32 = grad_y.astype(jnp.float32)
    x_buf = jnp.einsum(
        "tes,td->esd", rows_sel.astype(jnp.bfloat16), tokens, preferred_element_type=jnp.float32
    ).astype(jnp.bfloat16)
    g_buf = jnp.einsum("tes,td->esd", gate_sel, grad_f32, precision=highest).astype(jnp.bfloat16)
    flag = jnp.sum(gate_sel, axis=0)
    flag_cols = (jnp.arange(FLAG_COLS) == 0).astype(jnp.float32)
    flag_buf = (flag[:, :, None] * flag_cols).astype(jnp.bfloat16)
    send = jnp.concatenate([x_buf, g_buf, flag_buf], axis=-1)
    send = send.reshape(expert_devs, local_experts, slot_count, 2 * feature_dim + FLAG_COLS)
    mine = lax.axis_index("expert") * local_experts + jnp.arange(local_experts, dtype=jnp.int32)
    is_hot = jnp.any(mine[:, None] == hot_experts[None, :], axis=1)
    cap_mine = capacity[mine]
    backs, grads_wi, grads_wo = [], [], []
    for own in range(local_experts):
        recv = lax.all_to_all(send[:, own], "expert", split_axis=0, concat_axis=1, tiled=True)[0]
        valid = (recv[:, 2 * feature_dim] > 0).astype(jnp.int32)
        rank_of = jnp.cumsum(valid) - valid
        keep = (valid > 0) & (is_hot[own] | (rank_of < cap_mine[own]))
        rows = jnp.where(keep[:, None], recv[:, : 2 * feature_dim], jnp.zeros((), jnp.bfloat16))
        rows_all = lax.all_gather(rows, "dp", axis=0, tiled=False)[:, None]
        partial_terms, grad_wi, grad_wo = expert_math(
            rows_all[..., :feature_dim], rows_all[..., feature_dim:], w_in[own][None], w_out[own][None]
        )
        flat = partial_terms.reshape(-1, feature_dim)
        summed = lax.psum_scatter(flat, "dp", scatter_dimension=0, tiled=True)
        summed = summed.reshape(2, expert_devs, slot_count, feature_dim)
        backs.append(lax.all_to_all(summed, "expert", split_axis=1, concat_axis=1, tiled=True))
        grads_wi.append(grad_wi[0])
        grads_wo.append(grad_wo[0])
    back = jnp.stack(backs, axis=2).reshape(2, expert_total, slot_count, feature_dim)
    grad_wi = jnp.stack(grads_wi)
    grad_wo = jnp.stack(grads_wo)
    out_f32 = back[0].astype(jnp.float32)
    in_f32 = back[1].astype(jnp.float32)
    mixed = jnp.einsum("tes,esd->td", gate_sel, out_f32, precision=highest)
    token_grad = jnp.einsum("tes,esd->td", rows_sel, in_f32, precision=highest)
    dot_vals = jnp.einsum("td,esd->tes", grad_f32, out_f32, precision=highest)
    gate_grad = jnp.einsum("tkes,tes->tk", send_picks, dot_vals, precision=highest)
    return (
        mixed.astype(jnp.bfloat16),
        token_grad.astype(jnp.bfloat16),
        gate_grad,
        grad_wi.astype(jnp.bfloat16),
        grad_wo.astype(jnp.bfloat16),
    )


def solution(mesh):
    in_specs = (
        P(("dp", "expert"), None),
        P(("dp", "expert"), None),
        P(("dp", "expert"), None),
        P(),
        P(),
        P("expert", None, "dp"),
        P("expert", "dp", None),
        P(("dp", "expert"), None),
    )
    out_specs = (
        P(("dp", "expert"), None),
        P(("dp", "expert"), None),
        P(("dp", "expert"), None),
        P("expert", None, "dp"),
        P("expert", "dp", None),
    )
    return jax.shard_map(local, mesh=mesh, in_specs=in_specs, out_specs=out_specs, check_vma=False)
```

```python
import jax
import jax.numpy as jnp
from jax import lax
from jax.sharding import PartitionSpec as P


FLAG_COLS = 128
CAP_MAX = 64


def silu_terms(pre_act):
    sig_val = jax.nn.sigmoid(pre_act)
    return (pre_act * sig_val, sig_val * (1.0 + pre_act * (1.0 - sig_val)))


def expert_math(rows_x, rows_g, weight_in, weight_out):
    pre_act = jnp.einsum("gerd,edh->gerh", rows_x, weight_in, preferred_element_type=jnp.float32)
    act_full, slope_val = silu_terms(pre_act)
    act_low = act_full.astype(jnp.bfloat16)
    out_part = jnp.einsum("gerh,ehd->gerd", act_low, weight_out, preferred_element_type=jnp.float32)
    back_act = jnp.einsum("gerd,ehd->gerh", rows_g, weight_out, preferred_element_type=jnp.float32)
    pre_grad = (back_act * slope_val).astype(jnp.bfloat16)
    in_part = jnp.einsum("gerh,edh->gerd", pre_grad, weight_in, preferred_element_type=jnp.float32)
    grad_in = jnp.einsum("gerd,gerh->edh", rows_x, pre_grad, preferred_element_type=jnp.float32)
    grad_out = jnp.einsum("gerh,gerd->ehd", act_low, rows_g, preferred_element_type=jnp.float32)
    stacked = jnp.stack([out_part, in_part], axis=1)
    return (stacked.astype(jnp.bfloat16), grad_in, grad_out)


def local(tokens, expert_ids, gate_weights, hot_experts, capacity, w_in, w_out, grad_y):
    highest = lax.Precision.HIGHEST
    expert_devs = lax.axis_size("expert")
    tok_rows, top_k = expert_ids.shape
    local_experts = w_in.shape[0]
    expert_total = local_experts * expert_devs
    slot_count = max(2, 3 * tok_rows * top_k // (2 * expert_total))
    feature_dim = tokens.shape[1]
    labels = jnp.arange(expert_total, dtype=jnp.int32)
    name_hit = (expert_ids[:, :, None] == labels).astype(jnp.int32)
    per_token = jnp.sum(name_hit, axis=1)
    within_dev = jnp.cumsum(per_token, axis=0) - per_token
    slot_hit = (within_dev[:, :, None] == jnp.arange(slot_count, dtype=jnp.int32)).astype(
        jnp.float32
    )
    send_picks = name_hit.astype(jnp.float32)[:, :, :, None] * slot_hit[:, None, :, :]
    rows_sel = jnp.sum(send_picks, axis=1)
    gate_sel = jnp.einsum("tkes,tk->tes", send_picks, gate_weights, precision=highest)
    grad_f32 = grad_y.astype(jnp.float32)
    x_buf = jnp.einsum(
        "tes,td->esd", rows_sel.astype(jnp.bfloat16), tokens, preferred_element_type=jnp.float32
    ).astype(jnp.bfloat16)
    g_buf = jnp.einsum("tes,td->esd", gate_sel, grad_f32, precision=highest).astype(jnp.bfloat16)
    flag = jnp.sum(gate_sel, axis=0)
    flag_cols = (jnp.arange(FLAG_COLS) == 0).astype(jnp.float32)
    flag_buf = (flag[:, :, None] * flag_cols).astype(jnp.bfloat16)
    send = jnp.concatenate([x_buf, g_buf, flag_buf], axis=-1)
    send = send.reshape(expert_devs, local_experts, slot_count, 2 * feature_dim + FLAG_COLS)
    mine = lax.axis_index("expert") * local_experts + jnp.arange(local_experts, dtype=jnp.int32)
    is_hot = jnp.any(mine[:, None] == hot_experts[None, :], axis=1)
    cap_mine = capacity[mine]
    hot_all = jnp.any(labels[:, None] == hot_experts[None, :], axis=1).reshape(expert_devs, local_experts)
    hot_per_dev = jnp.sum(hot_all.astype(jnp.int32), axis=1)

    def chain(recv, weight_in, weight_out, hot_e, cap_e, compact):
        valid = (recv[:, 2 * feature_dim] > 0).astype(jnp.int32)
        rank_of = jnp.cumsum(valid) - valid
        keep = (valid > 0) & (hot_e | (rank_of < cap_e))
        rows = jnp.where(keep[:, None], recv[:, : 2 * feature_dim], jnp.zeros((), jnp.bfloat16))
        if compact:
            pick = keep[None, :] & (rank_of[None, :] == jnp.arange(CAP_MAX, dtype=jnp.int32)[:, None])
            pick = pick.astype(jnp.bfloat16)
            rows = jnp.dot(pick, rows, preferred_element_type=jnp.float32).astype(jnp.bfloat16)
        rows_all = lax.all_gather(rows, "dp", axis=0, tiled=False)[:, None]
        partial_terms, grad_wi, grad_wo = expert_math(
            rows_all[..., :feature_dim], rows_all[..., feature_dim:], weight_in[None], weight_out[None]
        )
        flat = partial_terms.reshape(-1, feature_dim)
        summed = lax.psum_scatter(flat, "dp", scatter_dimension=0, tiled=True)
        summed = summed.reshape(2, -1, feature_dim)
        if compact:
            summed = jnp.einsum(
                "kr,ckd->crd", pick, summed, preferred_element_type=jnp.float32
            ).astype(jnp.bfloat16)
        summed = summed.reshape(2, expert_devs, slot_count, feature_dim)
        back = lax.all_to_all(summed, "expert", split_axis=1, concat_axis=1, tiled=True)
        return back, grad_wi[0], grad_wo[0]

    def each_expert(send, w_in, w_out):
        backs, grads_wi, grads_wo = [], [], []
        for own in range(local_experts):
            recv = lax.all_to_all(send[:, own], "expert", split_axis=0, concat_axis=1, tiled=True)[0]
            back, grad_wi, grad_wo = chain(recv, w_in[own], w_out[own], is_hot[own], cap_mine[own], False)
            backs.append(back)
            grads_wi.append(grad_wi)
            grads_wo.append(grad_wo)
        return jnp.stack(backs, axis=2), jnp.stack(grads_wi), jnp.stack(grads_wo)

    def hot_first(send, w_in, w_out):
        first = jnp.argmax(hot_all, axis=1) == 0
        send_a = jnp.where(first[:, None, None], send[:, 0], send[:, 1])
        send_b = jnp.where(first[:, None, None], send[:, 1], send[:, 0])
        own_a = jnp.argmax(is_hot).astype(jnp.int32)
        own_b = 1 - own_a
        recv_a = lax.all_to_all(send_a, "expert", split_axis=0, concat_axis=1, tiled=True)[0]
        back_a, wi_a, wo_a = chain(recv_a, w_in[own_a], w_out[own_a], is_hot[own_a], cap_mine[own_a], False)
        recv_b = lax.all_to_all(send_b, "expert", split_axis=0, concat_axis=1, tiled=True)[0]
        back_b, wi_b, wo_b = chain(recv_b, w_in[own_b], w_out[own_b], is_hot[own_b], cap_mine[own_b], True)
        pick_first = first[None, :, None, None]
        back = jnp.stack(
            [jnp.where(pick_first, back_a, back_b), jnp.where(pick_first, back_b, back_a)], axis=2
        )
        mine_first = own_a == 0
        grad_wi = jnp.stack([jnp.where(mine_first, wi_a, wi_b), jnp.where(mine_first, wi_b, wi_a)])
        grad_wo = jnp.stack([jnp.where(mine_first, wo_a, wo_b), jnp.where(mine_first, wo_b, wo_a)])
        return back, grad_wi, grad_wo

    if local_experts == 2 and expert_devs * slot_count > CAP_MAX:
        one_hot_each = jnp.all(hot_per_dev <= 1)
        back, grad_wi, grad_wo = lax.cond(one_hot_each, hot_first, each_expert, send, w_in, w_out)
    else:
        back, grad_wi, grad_wo = each_expert(send, w_in, w_out)
    back = back.reshape(2, expert_total, slot_count, feature_dim)
    out_f32 = back[0].astype(jnp.float32)
    in_f32 = back[1].astype(jnp.float32)
    mixed = jnp.einsum("tes,esd->td", gate_sel, out_f32, precision=highest)
    token_grad = jnp.einsum("tes,esd->td", rows_sel, in_f32, precision=highest)
    dot_vals = jnp.einsum("td,esd->tes", grad_f32, out_f32, precision=highest)
    gate_grad = jnp.einsum("tkes,tes->tk", send_picks, dot_vals, precision=highest)
    return (
        mixed.astype(jnp.bfloat16),
        token_grad.astype(jnp.bfloat16),
        gate_grad,
        grad_wi.astype(jnp.bfloat16),
        grad_wo.astype(jnp.bfloat16),
    )


def solution(mesh):
    in_specs = (
        P(("dp", "expert"), None),
        P(("dp", "expert"), None),
        P(("dp", "expert"), None),
        P(),
        P(),
        P("expert", None, "dp"),
        P("expert", "dp", None),
        P(("dp", "expert"), None),
    )
    out_specs = (
        P(("dp", "expert"), None),
        P(("dp", "expert"), None),
        P(("dp", "expert"), None),
        P("expert", None, "dp"),
        P("expert", "dp", None),
    )
    return jax.shard_map(local, mesh=mesh, in_specs=in_specs, out_specs=out_specs, check_vma=False)
```

```python
from functools import partial

import jax
import jax.numpy as jnp
from jax import lax
from jax.sharding import PartitionSpec as P


FLAG_COLS = 128
CAP_MAX = 64


def silu_terms(pre_act):
    sig_val = jax.nn.sigmoid(pre_act)
    return (pre_act * sig_val, sig_val * (1.0 + pre_act * (1.0 - sig_val)))


def expert_math(rows_x, rows_g, weight_in, weight_out):
    pre_act = jnp.einsum("gerd,edh->gerh", rows_x, weight_in, preferred_element_type=jnp.float32)
    act_full, slope_val = silu_terms(pre_act)
    act_low = act_full.astype(jnp.bfloat16)
    out_part = jnp.einsum("gerh,ehd->gerd", act_low, weight_out, preferred_element_type=jnp.float32)
    back_act = jnp.einsum("gerd,ehd->gerh", rows_g, weight_out, preferred_element_type=jnp.float32)
    pre_grad = (back_act * slope_val).astype(jnp.bfloat16)
    in_part = jnp.einsum("gerh,edh->gerd", pre_grad, weight_in, preferred_element_type=jnp.float32)
    grad_in = jnp.einsum("gerd,gerh->edh", rows_x, pre_grad, preferred_element_type=jnp.float32)
    grad_out = jnp.einsum("gerh,gerd->ehd", act_low, rows_g, preferred_element_type=jnp.float32)
    stacked = jnp.stack([out_part, in_part], axis=1)
    return (stacked.astype(jnp.bfloat16), grad_in, grad_out)


def local(tokens, expert_ids, gate_weights, hot_experts, capacity, w_in, w_out, grad_y):
    highest = lax.Precision.HIGHEST
    expert_devs = lax.axis_size("expert")
    tok_rows, top_k = expert_ids.shape
    local_experts = w_in.shape[0]
    expert_total = local_experts * expert_devs
    slot_count = max(2, 3 * tok_rows * top_k // (2 * expert_total))
    feature_dim = tokens.shape[1]
    labels = jnp.arange(expert_total, dtype=jnp.int32)
    hot_all = jnp.any(labels[:, None] == hot_experts[None, :], axis=1).reshape(expert_devs, local_experts)
    hot_per_dev = jnp.sum(hot_all.astype(jnp.int32), axis=1)
    split_hot = local_experts == 2 and expert_devs * slot_count > CAP_MAX
    dev_base = jnp.arange(expert_devs, dtype=jnp.int32) * local_experts
    if split_hot:
        first_local = jnp.argmax(hot_all, axis=1).astype(jnp.int32)
        order = jnp.stack([dev_base + first_local, dev_base + 1 - first_local])
    else:
        order = dev_base[None, :] + jnp.arange(local_experts, dtype=jnp.int32)[:, None]
    order = order.reshape(expert_total)
    name_hit = (expert_ids[:, :, None] == order).astype(jnp.int32)
    per_token = jnp.sum(name_hit, axis=1)
    within_dev = jnp.cumsum(per_token, axis=0) - per_token
    slot_hit = (within_dev[:, :, None] == jnp.arange(slot_count, dtype=jnp.int32)).astype(
        jnp.float32
    )
    send_picks = name_hit.astype(jnp.float32)[:, :, :, None] * slot_hit[:, None, :, :]
    rows_sel = jnp.sum(send_picks, axis=1)
    gate_sel = jnp.einsum("tkes,tk->tes", send_picks, gate_weights, precision=highest)
    grad_f32 = grad_y.astype(jnp.float32)
    x_buf = jnp.einsum(
        "tes,td->esd", rows_sel.astype(jnp.bfloat16), tokens, preferred_element_type=jnp.float32
    ).astype(jnp.bfloat16)
    g_buf = jnp.einsum("tes,td->esd", gate_sel, grad_f32, precision=highest).astype(jnp.bfloat16)
    flag = jnp.sum(gate_sel, axis=0)
    flag_cols = (jnp.arange(FLAG_COLS) == 0).astype(jnp.float32)
    flag_buf = (flag[:, :, None] * flag_cols).astype(jnp.bfloat16)
    send = jnp.concatenate([x_buf, g_buf, flag_buf], axis=-1)
    send = send.reshape(local_experts, expert_devs, slot_count, 2 * feature_dim + FLAG_COLS)
    mine = lax.axis_index("expert") * local_experts + jnp.arange(local_experts, dtype=jnp.int32)
    is_hot = jnp.any(mine[:, None] == hot_experts[None, :], axis=1)
    cap_mine = capacity[mine]

    def chain(recv, weight_in, weight_out, hot_e, cap_e, compact):
        valid = (recv[:, 2 * feature_dim] > 0).astype(jnp.int32)
        rank_of = jnp.cumsum(valid) - valid
        keep = (valid > 0) & (hot_e | (rank_of < cap_e))
        rows = jnp.where(keep[:, None], recv[:, : 2 * feature_dim], jnp.zeros((), jnp.bfloat16))
        if compact:
            pick = keep[None, :] & (rank_of[None, :] == jnp.arange(CAP_MAX, dtype=jnp.int32)[:, None])
            pick = pick.astype(jnp.bfloat16)
            rows = jnp.dot(pick, rows, preferred_element_type=jnp.float32).astype(jnp.bfloat16)
        rows_all = lax.all_gather(rows, "dp", axis=0, tiled=False)[:, None]
        partial_terms, grad_wi, grad_wo = expert_math(
            rows_all[..., :feature_dim], rows_all[..., feature_dim:], weight_in[None], weight_out[None]
        )
        flat = partial_terms.reshape(-1, feature_dim)
        summed = lax.psum_scatter(flat, "dp", scatter_dimension=0, tiled=True)
        summed = summed.reshape(2, -1, feature_dim)
        if compact:
            summed = jnp.einsum(
                "kr,ckd->crd", pick, summed, preferred_element_type=jnp.float32
            ).astype(jnp.bfloat16)
        summed = summed.reshape(2, expert_devs, slot_count, feature_dim)
        back = lax.all_to_all(summed, "expert", split_axis=1, concat_axis=1, tiled=True)
        return back, grad_wi[0], grad_wo[0]

    if split_hot:
        own_a = jnp.argmax(is_hot).astype(jnp.int32)
        owns = [own_a, 1 - own_a]
    else:
        owns = list(range(local_experts))

    def run(compact_last, send, w_in, w_out):
        backs, grads_wi, grads_wo = [], [], []
        for chunk, own in enumerate(owns):
            recv = lax.all_to_all(send[chunk], "expert", split_axis=0, concat_axis=1, tiled=True)[0]
            compact = compact_last and chunk == len(owns) - 1
            back, grad_wi, grad_wo = chain(recv, w_in[own], w_out[own], is_hot[own], cap_mine[own], compact)
            backs.append(back)
            grads_wi.append(grad_wi)
            grads_wo.append(grad_wo)
        back = jnp.stack(backs, axis=1)
        if split_hot:
            first = owns[0] == 0
            grad_wi = jnp.stack([jnp.where(first, grads_wi[0], grads_wi[1]), jnp.where(first, grads_wi[1], grads_wi[0])])
            grad_wo = jnp.stack([jnp.where(first, grads_wo[0], grads_wo[1]), jnp.where(first, grads_wo[1], grads_wo[0])])
        else:
            grad_wi, grad_wo = jnp.stack(grads_wi), jnp.stack(grads_wo)
        return back, grad_wi, grad_wo

    if split_hot:
        one_hot_each = jnp.all(hot_per_dev <= 1)
        back, grad_wi, grad_wo = lax.cond(
            one_hot_each, partial(run, True), partial(run, False), send, w_in, w_out
        )
    else:
        back, grad_wi, grad_wo = run(False, send, w_in, w_out)
    back = back.reshape(2, expert_total, slot_count, feature_dim)
    out_f32 = back[0].astype(jnp.float32)
    in_f32 = back[1].astype(jnp.float32)
    mixed = jnp.einsum("tes,esd->td", gate_sel, out_f32, precision=highest)
    token_grad = jnp.einsum("tes,esd->td", rows_sel, in_f32, precision=highest)
    dot_vals = jnp.einsum("td,esd->tes", grad_f32, out_f32, precision=highest)
    gate_grad = jnp.einsum("tkes,tes->tk", send_picks, dot_vals, precision=highest)
    return (
        mixed.astype(jnp.bfloat16),
        token_grad.astype(jnp.bfloat16),
        gate_grad,
        grad_wi.astype(jnp.bfloat16),
        grad_wo.astype(jnp.bfloat16),
    )


def solution(mesh):
    in_specs = (
        P(("dp", "expert"), None),
        P(("dp", "expert"), None),
        P(("dp", "expert"), None),
        P(),
        P(),
        P("expert", None, "dp"),
        P("expert", "dp", None),
        P(("dp", "expert"), None),
    )
    out_specs = (
        P(("dp", "expert"), None),
        P(("dp", "expert"), None),
        P(("dp", "expert"), None),
        P("expert", None, "dp"),
        P("expert", "dp", None),
    )
    return jax.shard_map(local, mesh=mesh, in_specs=in_specs, out_specs=out_specs, check_vma=False)
```

```python
from functools import partial

import jax
import jax.numpy as jnp
from jax import lax
from jax.sharding import PartitionSpec as P


FLAG_COLS = 128
CAP_MAX = 64


def silu_terms(pre_act):
    sig_val = jax.nn.sigmoid(pre_act)
    return (pre_act * sig_val, sig_val * (1.0 + pre_act * (1.0 - sig_val)))


def expert_math(rows_x, rows_g, weight_in, weight_out):
    pre_act = jnp.einsum("gerd,edh->gerh", rows_x, weight_in, preferred_element_type=jnp.float32)
    act_full, slope_val = silu_terms(pre_act)
    act_low = act_full.astype(jnp.bfloat16)
    out_part = jnp.einsum("gerh,ehd->gerd", act_low, weight_out, preferred_element_type=jnp.float32)
    back_act = jnp.einsum("gerd,ehd->gerh", rows_g, weight_out, preferred_element_type=jnp.float32)
    pre_grad = (back_act * slope_val).astype(jnp.bfloat16)
    in_part = jnp.einsum("gerh,edh->gerd", pre_grad, weight_in, preferred_element_type=jnp.float32)
    grad_in = jnp.einsum("gerd,gerh->edh", rows_x, pre_grad, preferred_element_type=jnp.float32)
    grad_out = jnp.einsum("gerh,gerd->ehd", act_low, rows_g, preferred_element_type=jnp.float32)
    stacked = jnp.stack([out_part, in_part], axis=1)
    return (stacked.astype(jnp.bfloat16), grad_in, grad_out)


def local(tokens, expert_ids, gate_weights, hot_experts, capacity, w_in, w_out, grad_y):
    highest = lax.Precision.HIGHEST
    expert_devs = lax.axis_size("expert")
    tok_rows, top_k = expert_ids.shape
    local_experts = w_in.shape[0]
    expert_total = local_experts * expert_devs
    slot_count = max(2, 3 * tok_rows * top_k // (2 * expert_total))
    feature_dim = tokens.shape[1]
    labels = jnp.arange(expert_total, dtype=jnp.int32)
    hot_all = jnp.any(labels[:, None] == hot_experts[None, :], axis=1).reshape(expert_devs, local_experts)
    hot_per_dev = jnp.sum(hot_all.astype(jnp.int32), axis=1)
    split_hot = local_experts == 2 and expert_devs * slot_count > CAP_MAX
    dev_base = jnp.arange(expert_devs, dtype=jnp.int32) * local_experts
    if split_hot:
        first_local = jnp.argmax(hot_all, axis=1).astype(jnp.int32)
        order = jnp.stack([dev_base + first_local, dev_base + 1 - first_local])
    else:
        order = dev_base[None, :] + jnp.arange(local_experts, dtype=jnp.int32)[:, None]
    order = order.reshape(expert_total)
    name_hit = (expert_ids[:, :, None] == order).astype(jnp.int32)
    per_token = jnp.sum(name_hit, axis=1)
    within_dev = jnp.cumsum(per_token, axis=0) - per_token
    slot_hit = (within_dev[:, :, None] == jnp.arange(slot_count, dtype=jnp.int32)).astype(
        jnp.float32
    )
    send_picks = name_hit.astype(jnp.float32)[:, :, :, None] * slot_hit[:, None, :, :]
    rows_sel = jnp.sum(send_picks, axis=1)
    gate_sel = jnp.einsum("tkes,tk->tes", send_picks, gate_weights, precision=highest)
    grad_f32 = grad_y.astype(jnp.float32)
    x_buf = jnp.einsum(
        "tes,td->esd", rows_sel.astype(jnp.bfloat16), tokens, preferred_element_type=jnp.float32
    ).astype(jnp.bfloat16)
    g_buf = jnp.einsum("tes,td->esd", gate_sel, grad_f32, precision=highest).astype(jnp.bfloat16)
    flag = jnp.sum(gate_sel, axis=0)
    flag_cols = (jnp.arange(FLAG_COLS) == 0).astype(jnp.float32)
    flag_buf = (flag[:, :, None] * flag_cols).astype(jnp.bfloat16)
    send = jnp.concatenate([x_buf, g_buf, flag_buf], axis=-1)
    send = send.reshape(local_experts, expert_devs, slot_count, 2 * feature_dim + FLAG_COLS)
    mine = lax.axis_index("expert") * local_experts + jnp.arange(local_experts, dtype=jnp.int32)
    is_hot = jnp.any(mine[:, None] == hot_experts[None, :], axis=1)
    cap_mine = capacity[mine]

    def prepare(recv, hot_e, cap_e, compact):
        valid = (recv[:, 2 * feature_dim] > 0).astype(jnp.int32)
        rank_of = jnp.cumsum(valid) - valid
        keep = (valid > 0) & (hot_e | (rank_of < cap_e))
        rows = jnp.where(keep[:, None], recv[:, : 2 * feature_dim], jnp.zeros((), jnp.bfloat16))
        pick = None
        if compact:
            pick = keep[None, :] & (rank_of[None, :] == jnp.arange(CAP_MAX, dtype=jnp.int32)[:, None])
            pick = pick.astype(jnp.bfloat16)
            rows = jnp.dot(pick, rows, preferred_element_type=jnp.float32).astype(jnp.bfloat16)
        return rows, pick

    def compute(rows_all, weight_in, weight_out):
        rows_all = rows_all[:, None]
        partial_terms, grad_wi, grad_wo = expert_math(
            rows_all[..., :feature_dim], rows_all[..., feature_dim:], weight_in[None], weight_out[None]
        )
        return partial_terms.reshape(-1, feature_dim), grad_wi[0], grad_wo[0]

    def finish(flat, pick):
        summed = lax.psum_scatter(flat, "dp", scatter_dimension=0, tiled=True)
        summed = summed.reshape(2, -1, feature_dim)
        if pick is not None:
            summed = jnp.einsum(
                "kr,ckd->crd", pick, summed, preferred_element_type=jnp.float32
            ).astype(jnp.bfloat16)
        summed = summed.reshape(2, expert_devs, slot_count, feature_dim)
        return lax.all_to_all(summed, "expert", split_axis=1, concat_axis=1, tiled=True)

    if split_hot:
        own_a = jnp.argmax(is_hot).astype(jnp.int32)
        owns = [own_a, 1 - own_a]
    else:
        owns = list(range(local_experts))

    def run(compact_last, send, w_in, w_out):
        recvs = []
        for chunk in range(len(owns)):
            chunk_send = send[chunk]
            if recvs:
                chunk_send, recvs[-1] = lax.optimization_barrier((chunk_send, recvs[-1]))
            recvs.append(lax.all_to_all(chunk_send, "expert", split_axis=0, concat_axis=1, tiled=True)[0])
        gathered, picks = [], []
        for chunk, own in enumerate(owns):
            compact = compact_last and chunk == len(owns) - 1
            rows, pick = prepare(recvs[chunk], is_hot[own], cap_mine[own], compact)
            if gathered:
                rows, gathered[-1] = lax.optimization_barrier((rows, gathered[-1]))
            gathered.append(lax.all_gather(rows, "dp", axis=0, tiled=False))
            picks.append(pick)
        flats, grads_wi, grads_wo = [], [], []
        for chunk, own in enumerate(owns):
            rows_all = gathered[chunk]
            if flats:
                rows_all, flats[-1] = lax.optimization_barrier((rows_all, flats[-1]))
            flat, grad_wi, grad_wo = compute(rows_all, w_in[own], w_out[own])
            flats.append(flat)
            grads_wi.append(grad_wi)
            grads_wo.append(grad_wo)
        backs = [finish(flat, pick) for flat, pick in zip(flats, picks)]
        back = jnp.stack(backs, axis=1)
        if split_hot:
            first = owns[0] == 0
            grad_wi = jnp.stack([jnp.where(first, grads_wi[0], grads_wi[1]), jnp.where(first, grads_wi[1], grads_wi[0])])
            grad_wo = jnp.stack([jnp.where(first, grads_wo[0], grads_wo[1]), jnp.where(first, grads_wo[1], grads_wo[0])])
        else:
            grad_wi, grad_wo = jnp.stack(grads_wi), jnp.stack(grads_wo)
        return back, grad_wi, grad_wo

    if split_hot:
        one_hot_each = jnp.all(hot_per_dev <= 1)
        back, grad_wi, grad_wo = lax.cond(
            one_hot_each, partial(run, True), partial(run, False), send, w_in, w_out
        )
    else:
        back, grad_wi, grad_wo = run(False, send, w_in, w_out)
    back = back.reshape(2, expert_total, slot_count, feature_dim)
    out_f32 = back[0].astype(jnp.float32)
    in_f32 = back[1].astype(jnp.float32)
    mixed = jnp.einsum("tes,esd->td", gate_sel, out_f32, precision=highest)
    token_grad = jnp.einsum("tes,esd->td", rows_sel, in_f32, precision=highest)
    dot_vals = jnp.einsum("td,esd->tes", grad_f32, out_f32, precision=highest)
    gate_grad = jnp.einsum("tkes,tes->tk", send_picks, dot_vals, precision=highest)
    return (
        mixed.astype(jnp.bfloat16),
        token_grad.astype(jnp.bfloat16),
        gate_grad,
        grad_wi.astype(jnp.bfloat16),
        grad_wo.astype(jnp.bfloat16),
    )


def solution(mesh):
    in_specs = (
        P(("dp", "expert"), None),
        P(("dp", "expert"), None),
        P(("dp", "expert"), None),
        P(),
        P(),
        P("expert", None, "dp"),
        P("expert", "dp", None),
        P(("dp", "expert"), None),
    )
    out_specs = (
        P(("dp", "expert"), None),
        P(("dp", "expert"), None),
        P(("dp", "expert"), None),
        P("expert", None, "dp"),
        P("expert", "dp", None),
    )
    return jax.shard_map(local, mesh=mesh, in_specs=in_specs, out_specs=out_specs, check_vma=False)
```

```python
from functools import partial

import jax
import jax.numpy as jnp
from jax import lax
from jax.sharding import PartitionSpec as P


FLAG_COLS = 128
CAP_MAX = 64


def silu_terms(pre_act):
    sig_val = jax.nn.sigmoid(pre_act)
    return (pre_act * sig_val, sig_val * (1.0 + pre_act * (1.0 - sig_val)))


def expert_math(rows_x, rows_g, weight_in, weight_out):
    pre_act = jnp.einsum("gerd,edh->gerh", rows_x, weight_in, preferred_element_type=jnp.float32)
    act_full, slope_val = silu_terms(pre_act)
    act_low = act_full.astype(jnp.bfloat16)
    out_part = jnp.einsum("gerh,ehd->gerd", act_low, weight_out, preferred_element_type=jnp.float32)
    back_act = jnp.einsum("gerd,ehd->gerh", rows_g, weight_out, preferred_element_type=jnp.float32)
    pre_grad = (back_act * slope_val).astype(jnp.bfloat16)
    in_part = jnp.einsum("gerh,edh->gerd", pre_grad, weight_in, preferred_element_type=jnp.float32)
    grad_in = jnp.einsum("gerd,gerh->edh", rows_x, pre_grad, preferred_element_type=jnp.float32)
    grad_out = jnp.einsum("gerh,gerd->ehd", act_low, rows_g, preferred_element_type=jnp.float32)
    stacked = jnp.stack([out_part, in_part], axis=1)
    return (stacked.astype(jnp.bfloat16), grad_in, grad_out)


def local(tokens, expert_ids, gate_weights, hot_experts, capacity, w_in, w_out, grad_y):
    highest = lax.Precision.HIGHEST
    expert_devs = lax.axis_size("expert")
    tok_rows, top_k = expert_ids.shape
    local_experts = w_in.shape[0]
    expert_total = local_experts * expert_devs
    slot_count = max(2, 3 * tok_rows * top_k // (2 * expert_total))
    feature_dim = tokens.shape[1]
    labels = jnp.arange(expert_total, dtype=jnp.int32)
    hot_all = jnp.any(labels[:, None] == hot_experts[None, :], axis=1).reshape(expert_devs, local_experts)
    hot_per_dev = jnp.sum(hot_all.astype(jnp.int32), axis=1)
    split_hot = local_experts == 2 and expert_devs * slot_count > CAP_MAX
    dev_base = jnp.arange(expert_devs, dtype=jnp.int32) * local_experts
    if split_hot:
        first_local = jnp.argmax(hot_all, axis=1).astype(jnp.int32)
        order = jnp.stack([dev_base + first_local, dev_base + 1 - first_local])
    else:
        order = dev_base[None, :] + jnp.arange(local_experts, dtype=jnp.int32)[:, None]
    order = order.reshape(expert_total)
    name_hit = (expert_ids[:, :, None] == order).astype(jnp.int32)
    per_token = jnp.sum(name_hit, axis=1)
    within_dev = jnp.cumsum(per_token, axis=0) - per_token
    slot_hit = (within_dev[:, :, None] == jnp.arange(slot_count, dtype=jnp.int32)).astype(
        jnp.float32
    )
    send_picks = name_hit.astype(jnp.float32)[:, :, :, None] * slot_hit[:, None, :, :]
    rows_sel = jnp.sum(send_picks, axis=1)
    gate_sel = jnp.einsum("tkes,tk->tes", send_picks, gate_weights, precision=highest)
    grad_f32 = grad_y.astype(jnp.float32)
    x_buf = jnp.einsum(
        "tes,td->esd", rows_sel.astype(jnp.bfloat16), tokens, preferred_element_type=jnp.float32
    ).astype(jnp.bfloat16)
    g_buf = jnp.einsum("tes,td->esd", gate_sel, grad_f32, precision=highest).astype(jnp.bfloat16)
    flag = jnp.sum(gate_sel, axis=0)
    flag_cols = (jnp.arange(FLAG_COLS) == 0).astype(jnp.float32)
    flag_buf = (flag[:, :, None] * flag_cols).astype(jnp.bfloat16)
    send = jnp.concatenate([x_buf, g_buf, flag_buf], axis=-1)
    send = send.reshape(local_experts, expert_devs, slot_count, 2 * feature_dim + FLAG_COLS)
    mine = lax.axis_index("expert") * local_experts + jnp.arange(local_experts, dtype=jnp.int32)
    is_hot = jnp.any(mine[:, None] == hot_experts[None, :], axis=1)
    cap_mine = capacity[mine]

    def prepare(recv, hot_e, cap_e, compact):
        valid = (recv[:, 2 * feature_dim] > 0).astype(jnp.int32)
        rank_of = jnp.cumsum(valid) - valid
        keep = (valid > 0) & (hot_e | (rank_of < cap_e))
        rows = jnp.where(keep[:, None], recv[:, : 2 * feature_dim], jnp.zeros((), jnp.bfloat16))
        pick = None
        if compact:
            pick = keep[None, :] & (rank_of[None, :] == jnp.arange(CAP_MAX, dtype=jnp.int32)[:, None])
            pick = pick.astype(jnp.bfloat16)
            rows = jnp.dot(pick, rows, preferred_element_type=jnp.float32).astype(jnp.bfloat16)
        return rows, pick

    def compute(rows_all, weight_in, weight_out):
        rows_all = rows_all[:, None]
        partial_terms, grad_wi, grad_wo = expert_math(
            rows_all[..., :feature_dim], rows_all[..., feature_dim:], weight_in[None], weight_out[None]
        )
        return partial_terms.reshape(-1, feature_dim), grad_wi[0], grad_wo[0]

    def reduce(flat):
        return lax.psum_scatter(flat, "dp", scatter_dimension=0, tiled=True)

    def finish(summed, pick):
        summed = summed.reshape(2, -1, feature_dim)
        if pick is not None:
            summed = jnp.einsum(
                "kr,ckd->crd", pick, summed, preferred_element_type=jnp.float32
            ).astype(jnp.bfloat16)
        summed = summed.reshape(2, expert_devs, slot_count, feature_dim)
        return lax.all_to_all(summed, "expert", split_axis=1, concat_axis=1, tiled=True)

    if split_hot:
        own_a = jnp.argmax(is_hot).astype(jnp.int32)
        owns = [own_a, 1 - own_a]
    else:
        owns = list(range(local_experts))

    def run(compact_last, send, w_in, w_out):
        recvs = []
        for chunk in range(len(owns)):
            chunk_send = send[chunk]
            if recvs:
                chunk_send, recvs[-1] = lax.optimization_barrier((chunk_send, recvs[-1]))
            recvs.append(lax.all_to_all(chunk_send, "expert", split_axis=0, concat_axis=1, tiled=True)[0])
        gathered, picks = [], []
        for chunk, own in enumerate(owns):
            compact = compact_last and chunk == len(owns) - 1
            rows, pick = prepare(recvs[chunk], is_hot[own], cap_mine[own], compact)
            if gathered:
                rows, gathered[-1] = lax.optimization_barrier((rows, gathered[-1]))
            gathered.append(lax.all_gather(rows, "dp", axis=0, tiled=False))
            picks.append(pick)
        flats, grads_wi, grads_wo = [], [], []
        for chunk, own in enumerate(owns):
            rows_all = gathered[chunk]
            if flats:
                rows_all, flats[-1] = lax.optimization_barrier((rows_all, flats[-1]))
            flat, grad_wi, grad_wo = compute(rows_all, w_in[own], w_out[own])
            flats.append(flat)
            grads_wi.append(grad_wi)
            grads_wo.append(grad_wo)
        sums = []
        for flat in flats:
            if sums:
                flat, sums[-1] = lax.optimization_barrier((flat, sums[-1]))
            sums.append(reduce(flat))
        backs = [finish(summed, pick) for summed, pick in zip(sums, picks)]
        back = jnp.stack(backs, axis=1)
        if split_hot:
            first = owns[0] == 0
            grad_wi = jnp.stack([jnp.where(first, grads_wi[0], grads_wi[1]), jnp.where(first, grads_wi[1], grads_wi[0])])
            grad_wo = jnp.stack([jnp.where(first, grads_wo[0], grads_wo[1]), jnp.where(first, grads_wo[1], grads_wo[0])])
        else:
            grad_wi, grad_wo = jnp.stack(grads_wi), jnp.stack(grads_wo)
        return back, grad_wi, grad_wo

    if split_hot:
        one_hot_each = jnp.all(hot_per_dev <= 1)
        back, grad_wi, grad_wo = lax.cond(
            one_hot_each, partial(run, True), partial(run, False), send, w_in, w_out
        )
    else:
        back, grad_wi, grad_wo = run(False, send, w_in, w_out)
    back = back.reshape(2, expert_total, slot_count, feature_dim)
    out_f32 = back[0].astype(jnp.float32)
    in_f32 = back[1].astype(jnp.float32)
    mixed = jnp.einsum("tes,esd->td", gate_sel, out_f32, precision=highest)
    token_grad = jnp.einsum("tes,esd->td", rows_sel, in_f32, precision=highest)
    dot_vals = jnp.einsum("td,esd->tes", grad_f32, out_f32, precision=highest)
    gate_grad = jnp.einsum("tkes,tes->tk", send_picks, dot_vals, precision=highest)
    return (
        mixed.astype(jnp.bfloat16),
        token_grad.astype(jnp.bfloat16),
        gate_grad,
        grad_wi.astype(jnp.bfloat16),
        grad_wo.astype(jnp.bfloat16),
    )


def solution(mesh):
    in_specs = (
        P(("dp", "expert"), None),
        P(("dp", "expert"), None),
        P(("dp", "expert"), None),
        P(),
        P(),
        P("expert", None, "dp"),
        P("expert", "dp", None),
        P(("dp", "expert"), None),
    )
    out_specs = (
        P(("dp", "expert"), None),
        P(("dp", "expert"), None),
        P(("dp", "expert"), None),
        P("expert", None, "dp"),
        P("expert", "dp", None),
    )
    return jax.shard_map(local, mesh=mesh, in_specs=in_specs, out_specs=out_specs, check_vma=False)
```

```python
from functools import partial

import jax
import jax.numpy as jnp
from jax import lax
from jax.sharding import PartitionSpec as P


FLAG_COLS = 128
CAP_MAX = 64


def silu_terms(pre_act):
    sig_val = jax.nn.sigmoid(pre_act)
    return (pre_act * sig_val, sig_val * (1.0 + pre_act * (1.0 - sig_val)))


def expert_math(rows_x, rows_g, weight_in, weight_out):
    pre_act = jnp.einsum("gerd,edh->gerh", rows_x, weight_in, preferred_element_type=jnp.float32)
    act_full, slope_val = silu_terms(pre_act)
    act_low = act_full.astype(jnp.bfloat16)
    out_part = jnp.einsum("gerh,ehd->gerd", act_low, weight_out, preferred_element_type=jnp.float32)
    back_act = jnp.einsum("gerd,ehd->gerh", rows_g, weight_out, preferred_element_type=jnp.float32)
    pre_grad = (back_act * slope_val).astype(jnp.bfloat16)
    in_part = jnp.einsum("gerh,edh->gerd", pre_grad, weight_in, preferred_element_type=jnp.float32)
    grad_in = jnp.einsum("gerd,gerh->edh", rows_x, pre_grad, preferred_element_type=jnp.float32)
    grad_out = jnp.einsum("gerh,gerd->ehd", act_low, rows_g, preferred_element_type=jnp.float32)
    stacked = jnp.stack([out_part, in_part], axis=1)
    return (stacked.astype(jnp.bfloat16), grad_in, grad_out)


def local(tokens, expert_ids, gate_weights, hot_experts, capacity, w_in, w_out, grad_y):
    highest = lax.Precision.HIGHEST
    expert_devs = lax.axis_size("expert")
    tok_rows, top_k = expert_ids.shape
    local_experts = w_in.shape[0]
    expert_total = local_experts * expert_devs
    slot_count = max(2, 3 * tok_rows * top_k // (2 * expert_total))
    feature_dim = tokens.shape[1]
    labels = jnp.arange(expert_total, dtype=jnp.int32)
    hot_all = jnp.any(labels[:, None] == hot_experts[None, :], axis=1).reshape(expert_devs, local_experts)
    hot_per_dev = jnp.sum(hot_all.astype(jnp.int32), axis=1)
    split_hot = local_experts == 2 and expert_devs * slot_count > CAP_MAX
    dev_base = jnp.arange(expert_devs, dtype=jnp.int32) * local_experts
    if split_hot:
        first_local = jnp.argmax(hot_all, axis=1).astype(jnp.int32)
        order = jnp.stack([dev_base + first_local, dev_base + 1 - first_local])
    else:
        order = dev_base[None, :] + jnp.arange(local_experts, dtype=jnp.int32)[:, None]
    order = order.reshape(expert_total)
    name_hit = (expert_ids[:, :, None] == order).astype(jnp.int32)
    per_token = jnp.sum(name_hit, axis=1)
    within_dev = jnp.cumsum(per_token, axis=0) - per_token
    slot_hit = (within_dev[:, :, None] == jnp.arange(slot_count, dtype=jnp.int32)).astype(
        jnp.float32
    )
    send_picks = name_hit.astype(jnp.float32)[:, :, :, None] * slot_hit[:, None, :, :]
    rows_sel = jnp.sum(send_picks, axis=1)
    gate_sel = jnp.einsum("tkes,tk->tes", send_picks, gate_weights, precision=highest)
    grad_f32 = grad_y.astype(jnp.float32)
    x_buf = jnp.einsum(
        "tes,td->esd", rows_sel.astype(jnp.bfloat16), tokens, preferred_element_type=jnp.float32
    ).astype(jnp.bfloat16)
    g_buf = jnp.einsum("tes,td->esd", gate_sel, grad_f32, precision=highest).astype(jnp.bfloat16)
    flag = jnp.sum(gate_sel, axis=0)
    flag_cols = (jnp.arange(FLAG_COLS) == 0).astype(jnp.float32)
    flag_buf = (flag[:, :, None] * flag_cols).astype(jnp.bfloat16)
    send = jnp.concatenate([x_buf, g_buf, flag_buf], axis=-1)
    send = send.reshape(local_experts, expert_devs, slot_count, 2 * feature_dim + FLAG_COLS)
    mine = lax.axis_index("expert") * local_experts + jnp.arange(local_experts, dtype=jnp.int32)
    is_hot = jnp.any(mine[:, None] == hot_experts[None, :], axis=1)
    cap_mine = capacity[mine]

    def prepare(recv, hot_e, cap_e, compact):
        valid = (recv[:, 2 * feature_dim] > 0).astype(jnp.int32)
        rank_of = jnp.cumsum(valid) - valid
        keep = (valid > 0) & (hot_e | (rank_of < cap_e))
        rows = jnp.where(keep[:, None], recv[:, : 2 * feature_dim], jnp.zeros((), jnp.bfloat16))
        pick = None
        if compact:
            pick = keep[None, :] & (rank_of[None, :] == jnp.arange(CAP_MAX, dtype=jnp.int32)[:, None])
            pick = pick.astype(jnp.bfloat16)
            rows = jnp.dot(pick, rows, preferred_element_type=jnp.float32).astype(jnp.bfloat16)
        return rows, pick

    def compute(rows_all, weight_in, weight_out):
        rows_all = rows_all[:, None]
        partial_terms, grad_wi, grad_wo = expert_math(
            rows_all[..., :feature_dim], rows_all[..., feature_dim:], weight_in[None], weight_out[None]
        )
        return partial_terms.reshape(-1, feature_dim), grad_wi[0], grad_wo[0]

    def reduce(flat):
        return lax.psum_scatter(flat, "dp", scatter_dimension=0, tiled=True)

    def finish(summed, pick):
        summed = summed.reshape(2, -1, feature_dim)
        if pick is not None:
            summed = jnp.einsum(
                "kr,ckd->crd", pick, summed, preferred_element_type=jnp.float32
            ).astype(jnp.bfloat16)
        summed = summed.reshape(2, expert_devs, slot_count, feature_dim)
        return lax.all_to_all(summed, "expert", split_axis=1, concat_axis=1, tiled=True)

    if split_hot:
        own_a = jnp.argmax(is_hot).astype(jnp.int32)
        owns = [own_a, 1 - own_a]
    else:
        owns = list(range(local_experts))

    def run(compact_last, send, w_in, w_out):
        recvs = []
        for chunk in range(len(owns)):
            chunk_send = send[chunk]
            if recvs:
                chunk_send, recvs[-1] = lax.optimization_barrier((chunk_send, recvs[-1]))
            recvs.append(lax.all_to_all(chunk_send, "expert", split_axis=0, concat_axis=1, tiled=True)[0])
        gathered, picks = [], []
        for chunk, own in enumerate(owns):
            compact = compact_last and chunk == len(owns) - 1
            rows, pick = prepare(recvs[chunk], is_hot[own], cap_mine[own], compact)
            if gathered:
                rows, gathered[-1] = lax.optimization_barrier((rows, gathered[-1]))
            gathered.append(lax.all_gather(rows, "dp", axis=0, tiled=False))
            picks.append(pick)
        flats, grads_wi, grads_wo = [], [], []
        for chunk, own in enumerate(owns):
            rows_all = gathered[chunk]
            if flats:
                rows_all, flats[-1] = lax.optimization_barrier((rows_all, flats[-1]))
            flat, grad_wi, grad_wo = compute(rows_all, w_in[own], w_out[own])
            flats.append(flat)
            grads_wi.append(grad_wi)
            grads_wo.append(grad_wo)
        sums = []
        for flat in flats:
            if sums:
                flat, sums[-1] = lax.optimization_barrier((flat, sums[-1]))
            sums.append(reduce(flat))
        backs = [finish(summed, pick) for summed, pick in zip(sums, picks)]
        back = tuple(backs)
        if split_hot:
            first = owns[0] == 0
            grad_wi = jnp.stack([jnp.where(first, grads_wi[0], grads_wi[1]), jnp.where(first, grads_wi[1], grads_wi[0])])
            grad_wo = jnp.stack([jnp.where(first, grads_wo[0], grads_wo[1]), jnp.where(first, grads_wo[1], grads_wo[0])])
        else:
            grad_wi, grad_wo = jnp.stack(grads_wi), jnp.stack(grads_wo)
        return back, grad_wi, grad_wo

    if split_hot:
        one_hot_each = jnp.all(hot_per_dev <= 1)
        back, grad_wi, grad_wo = lax.cond(
            one_hot_each, partial(run, True), partial(run, False), send, w_in, w_out
        )
    else:
        back, grad_wi, grad_wo = run(False, send, w_in, w_out)
    chunks = len(back)
    gate_c = gate_sel.reshape(tok_rows, chunks, expert_devs, slot_count)
    rows_c = rows_sel.reshape(tok_rows, chunks, expert_devs, slot_count)
    picks_c = send_picks.reshape(tok_rows, top_k, chunks, expert_devs, slot_count)
    mixed, token_grad, gate_grad = 0.0, 0.0, 0.0
    for chunk in range(chunks):
        out_f32 = back[chunk][0].astype(jnp.float32)
        in_f32 = back[chunk][1].astype(jnp.float32)
        mixed = mixed + jnp.einsum("tes,esd->td", gate_c[:, chunk], out_f32, precision=highest)
        token_grad = token_grad + jnp.einsum("tes,esd->td", rows_c[:, chunk], in_f32, precision=highest)
        dot_vals = jnp.einsum("td,esd->tes", grad_f32, out_f32, precision=highest)
        gate_grad = gate_grad + jnp.einsum("tkes,tes->tk", picks_c[:, :, chunk], dot_vals, precision=highest)
    return (
        mixed.astype(jnp.bfloat16),
        token_grad.astype(jnp.bfloat16),
        gate_grad,
        grad_wi.astype(jnp.bfloat16),
        grad_wo.astype(jnp.bfloat16),
    )


def solution(mesh):
    in_specs = (
        P(("dp", "expert"), None),
        P(("dp", "expert"), None),
        P(("dp", "expert"), None),
        P(),
        P(),
        P("expert", None, "dp"),
        P("expert", "dp", None),
        P(("dp", "expert"), None),
    )
    out_specs = (
        P(("dp", "expert"), None),
        P(("dp", "expert"), None),
        P(("dp", "expert"), None),
        P("expert", None, "dp"),
        P("expert", "dp", None),
    )
    return jax.shard_map(local, mesh=mesh, in_specs=in_specs, out_specs=out_specs, check_vma=False)
```

```python
from functools import partial

import jax
import jax.numpy as jnp
from jax import lax
from jax.sharding import PartitionSpec as P


FLAG_COLS = 128
CAP_MAX = 64


def silu_terms(pre_act):
    sig_val = jax.nn.sigmoid(pre_act)
    return (pre_act * sig_val, sig_val * (1.0 + pre_act * (1.0 - sig_val)))


def expert_math(rows_x, rows_g, weight_in, weight_out):
    pre_act = jnp.einsum("gerd,edh->gerh", rows_x, weight_in, preferred_element_type=jnp.float32)
    act_full, slope_val = silu_terms(pre_act)
    act_low = act_full.astype(jnp.bfloat16)
    out_part = jnp.einsum("gerh,ehd->gerd", act_low, weight_out, preferred_element_type=jnp.float32)
    back_act = jnp.einsum("gerd,ehd->gerh", rows_g, weight_out, preferred_element_type=jnp.float32)
    pre_grad = (back_act * slope_val).astype(jnp.bfloat16)
    in_part = jnp.einsum("gerh,edh->gerd", pre_grad, weight_in, preferred_element_type=jnp.float32)
    grad_in = jnp.einsum("gerd,gerh->edh", rows_x, pre_grad, preferred_element_type=jnp.float32)
    grad_out = jnp.einsum("gerh,gerd->ehd", act_low, rows_g, preferred_element_type=jnp.float32)
    stacked = jnp.stack([out_part, in_part], axis=1)
    return (stacked.astype(jnp.bfloat16), grad_in, grad_out)


def local(tokens, expert_ids, gate_weights, hot_experts, capacity, w_in, w_out, grad_y):
    highest = lax.Precision.HIGHEST
    expert_devs = lax.axis_size("expert")
    tok_rows, top_k = expert_ids.shape
    local_experts = w_in.shape[0]
    expert_total = local_experts * expert_devs
    slot_count = max(2, 3 * tok_rows * top_k // (2 * expert_total))
    feature_dim = tokens.shape[1]
    labels = jnp.arange(expert_total, dtype=jnp.int32)
    hot_all = jnp.any(labels[:, None] == hot_experts[None, :], axis=1).reshape(expert_devs, local_experts)
    hot_per_dev = jnp.sum(hot_all.astype(jnp.int32), axis=1)
    split_hot = local_experts == 2 and expert_devs * slot_count > CAP_MAX
    dev_base = jnp.arange(expert_devs, dtype=jnp.int32) * local_experts
    if split_hot:
        first_local = jnp.argmax(hot_all, axis=1).astype(jnp.int32)
        order = jnp.stack([dev_base + first_local, dev_base + 1 - first_local])
    else:
        order = dev_base[None, :] + jnp.arange(local_experts, dtype=jnp.int32)[:, None]
    order = order.reshape(expert_total)
    name_hit = (expert_ids[:, :, None] == order).astype(jnp.int32)
    per_token = jnp.sum(name_hit, axis=1)
    within_dev = jnp.cumsum(per_token, axis=0) - per_token
    slot_hit = (within_dev[:, :, None] == jnp.arange(slot_count, dtype=jnp.int32)).astype(
        jnp.float32
    )
    send_picks = name_hit.astype(jnp.float32)[:, :, :, None] * slot_hit[:, None, :, :]
    rows_sel = jnp.sum(send_picks, axis=1)
    gate_sel = jnp.einsum("tkes,tk->tes", send_picks, gate_weights, precision=highest)
    grad_f32 = grad_y.astype(jnp.float32)
    x_buf = jnp.einsum(
        "tes,td->esd", rows_sel.astype(jnp.bfloat16), tokens, preferred_element_type=jnp.float32
    ).astype(jnp.bfloat16)
    g_buf = jnp.einsum("tes,td->esd", gate_sel, grad_f32, precision=highest).astype(jnp.bfloat16)
    flag = jnp.sum(gate_sel, axis=0)
    flag_cols = (jnp.arange(FLAG_COLS) == 0).astype(jnp.float32)
    flag_buf = (flag[:, :, None] * flag_cols).astype(jnp.bfloat16)
    send = jnp.concatenate([x_buf, g_buf, flag_buf], axis=-1)
    send = send.reshape(local_experts, expert_devs, slot_count, 2 * feature_dim + FLAG_COLS)
    mine = lax.axis_index("expert") * local_experts + jnp.arange(local_experts, dtype=jnp.int32)
    is_hot = jnp.any(mine[:, None] == hot_experts[None, :], axis=1)
    cap_mine = capacity[mine]

    def prepare(recv, hot_e, cap_e, compact):
        valid = (recv[:, 2 * feature_dim] > 0).astype(jnp.int32)
        rank_of = jnp.cumsum(valid) - valid
        keep = (valid > 0) & (hot_e | (rank_of < cap_e))
        rows = jnp.where(keep[:, None], recv[:, : 2 * feature_dim], jnp.zeros((), jnp.bfloat16))
        pick = None
        if compact:
            pick = keep[None, :] & (rank_of[None, :] == jnp.arange(CAP_MAX, dtype=jnp.int32)[:, None])
            pick = pick.astype(jnp.bfloat16)
            rows = jnp.dot(pick, rows, preferred_element_type=jnp.float32).astype(jnp.bfloat16)
        return rows, pick

    def compute(rows_all, weight_in, weight_out):
        rows_all = rows_all[:, None]
        partial_terms, grad_wi, grad_wo = expert_math(
            rows_all[..., :feature_dim], rows_all[..., feature_dim:], weight_in[None], weight_out[None]
        )
        return partial_terms.reshape(-1, feature_dim), grad_wi[0], grad_wo[0]

    def reduce(flat):
        return lax.psum_scatter(flat, "dp", scatter_dimension=0, tiled=True)

    def finish(summed, pick):
        summed = summed.reshape(2, -1, feature_dim)
        if pick is not None:
            summed = jnp.einsum(
                "kr,ckd->crd", pick, summed, preferred_element_type=jnp.float32
            ).astype(jnp.bfloat16)
        summed = summed.reshape(2, expert_devs, slot_count, feature_dim)
        return lax.all_to_all(summed, "expert", split_axis=1, concat_axis=1, tiled=True)

    if split_hot:
        own_a = jnp.argmax(is_hot).astype(jnp.int32)
        owns = [own_a, 1 - own_a]
    else:
        owns = list(range(local_experts))

    def run(compact_last, send, w_in, w_out):
        recvs = []
        for chunk in range(len(owns)):
            chunk_send = send[chunk]
            if recvs:
                chunk_send, recvs[-1] = lax.optimization_barrier((chunk_send, recvs[-1]))
            recvs.append(lax.all_to_all(chunk_send, "expert", split_axis=0, concat_axis=1, tiled=True)[0])
        gathered, picks = [], []
        for chunk, own in enumerate(owns):
            compact = compact_last and chunk == len(owns) - 1
            rows, pick = prepare(recvs[chunk], is_hot[own], cap_mine[own], compact)
            if gathered:
                rows, gathered[-1] = lax.optimization_barrier((rows, gathered[-1]))
            gathered.append(lax.all_gather(rows, "dp", axis=0, tiled=False))
            picks.append(pick)
        flats, grads_wi, grads_wo = [], [], []
        for chunk, own in enumerate(owns):
            rows_all = gathered[chunk]
            if flats:
                rows_all, flats[-1] = lax.optimization_barrier((rows_all, flats[-1]))
            flat, grad_wi, grad_wo = compute(rows_all, w_in[own], w_out[own])
            flats.append(flat)
            grads_wi.append(grad_wi)
            grads_wo.append(grad_wo)
        sums = []
        for flat in flats:
            if sums:
                flat, sums[-1] = lax.optimization_barrier((flat, sums[-1]))
            sums.append(reduce(flat))
        backs = [finish(summed, pick) for summed, pick in zip(sums, picks)]
        back = tuple(backs)
        if split_hot:
            first = owns[0] == 0
            grad_wi = jnp.stack([jnp.where(first, grads_wi[0], grads_wi[1]), jnp.where(first, grads_wi[1], grads_wi[0])])
            grad_wo = jnp.stack([jnp.where(first, grads_wo[0], grads_wo[1]), jnp.where(first, grads_wo[1], grads_wo[0])])
        else:
            grad_wi, grad_wo = jnp.stack(grads_wi), jnp.stack(grads_wo)
        return back, grad_wi, grad_wo

    send_chunks = tuple(send[chunk] for chunk in range(local_experts))
    if split_hot:
        one_hot_each = jnp.all(hot_per_dev <= 1)
        back, grad_wi, grad_wo = lax.cond(
            one_hot_each, partial(run, True), partial(run, False), send_chunks, w_in, w_out
        )
    else:
        back, grad_wi, grad_wo = run(False, send_chunks, w_in, w_out)
    chunks = len(back)
    gate_c = gate_sel.reshape(tok_rows, chunks, expert_devs, slot_count)
    rows_c = rows_sel.reshape(tok_rows, chunks, expert_devs, slot_count)
    picks_c = send_picks.reshape(tok_rows, top_k, chunks, expert_devs, slot_count)
    mixed, token_grad, gate_grad = 0.0, 0.0, 0.0
    for chunk in range(chunks):
        out_f32 = back[chunk][0].astype(jnp.float32)
        in_f32 = back[chunk][1].astype(jnp.float32)
        mixed = mixed + jnp.einsum("tes,esd->td", gate_c[:, chunk], out_f32, precision=highest)
        token_grad = token_grad + jnp.einsum("tes,esd->td", rows_c[:, chunk], in_f32, precision=highest)
        dot_vals = jnp.einsum("td,esd->tes", grad_f32, out_f32, precision=highest)
        gate_grad = gate_grad + jnp.einsum("tkes,tes->tk", picks_c[:, :, chunk], dot_vals, precision=highest)
    return (
        mixed.astype(jnp.bfloat16),
        token_grad.astype(jnp.bfloat16),
        gate_grad,
        grad_wi.astype(jnp.bfloat16),
        grad_wo.astype(jnp.bfloat16),
    )


def solution(mesh):
    in_specs = (
        P(("dp", "expert"), None),
        P(("dp", "expert"), None),
        P(("dp", "expert"), None),
        P(),
        P(),
        P("expert", None, "dp"),
        P("expert", "dp", None),
        P(("dp", "expert"), None),
    )
    out_specs = (
        P(("dp", "expert"), None),
        P(("dp", "expert"), None),
        P(("dp", "expert"), None),
        P("expert", None, "dp"),
        P("expert", "dp", None),
    )
    return jax.shard_map(local, mesh=mesh, in_specs=in_specs, out_specs=out_specs, check_vma=False)
```

```python
from functools import partial

import jax
import jax.numpy as jnp
from jax import lax
from jax.sharding import PartitionSpec as P


FLAG_COLS = 128
CAP_MAX = 64


def silu_terms(pre_act):
    sig_val = jax.nn.sigmoid(pre_act)
    return (pre_act * sig_val, sig_val * (1.0 + pre_act * (1.0 - sig_val)))


def expert_math(rows_x, rows_g, weight_in, weight_out):
    pre_act = jnp.einsum("gerd,edh->gerh", rows_x, weight_in, preferred_element_type=jnp.float32)
    act_full, slope_val = silu_terms(pre_act)
    act_low = act_full.astype(jnp.bfloat16)
    out_part = jnp.einsum("gerh,ehd->gerd", act_low, weight_out, preferred_element_type=jnp.float32)
    back_act = jnp.einsum("gerd,ehd->gerh", rows_g, weight_out, preferred_element_type=jnp.float32)
    pre_grad = (back_act * slope_val).astype(jnp.bfloat16)
    in_part = jnp.einsum("gerh,edh->gerd", pre_grad, weight_in, preferred_element_type=jnp.float32)
    grad_in = jnp.einsum("gerd,gerh->edh", rows_x, pre_grad, preferred_element_type=jnp.float32)
    grad_out = jnp.einsum("gerh,gerd->ehd", act_low, rows_g, preferred_element_type=jnp.float32)
    stacked = jnp.stack([out_part, in_part], axis=1)
    return (stacked.astype(jnp.bfloat16), grad_in, grad_out)


def local(tokens, expert_ids, gate_weights, hot_experts, capacity, w_in, w_out, grad_y):
    highest = lax.Precision.HIGHEST
    expert_devs = lax.axis_size("expert")
    tok_rows, top_k = expert_ids.shape
    local_experts = w_in.shape[0]
    expert_total = local_experts * expert_devs
    slot_count = max(2, 3 * tok_rows * top_k // (2 * expert_total))
    feature_dim = tokens.shape[1]
    labels = jnp.arange(expert_total, dtype=jnp.int32)
    hot_all = jnp.any(labels[:, None] == hot_experts[None, :], axis=1).reshape(expert_devs, local_experts)
    hot_per_dev = jnp.sum(hot_all.astype(jnp.int32), axis=1)
    split_hot = local_experts == 2 and expert_devs * slot_count > CAP_MAX
    dev_base = jnp.arange(expert_devs, dtype=jnp.int32) * local_experts
    if split_hot:
        first_local = jnp.argmax(hot_all, axis=1).astype(jnp.int32)
        order = jnp.stack([dev_base + first_local, dev_base + 1 - first_local])
    else:
        order = dev_base[None, :] + jnp.arange(local_experts, dtype=jnp.int32)[:, None]
    order = order.reshape(expert_total)
    name_hit = (expert_ids[:, :, None] == order).astype(jnp.int32)
    per_token = jnp.sum(name_hit, axis=1)
    within_dev = jnp.cumsum(per_token, axis=0) - per_token
    slot_hit = (within_dev[:, :, None] == jnp.arange(slot_count, dtype=jnp.int32)).astype(
        jnp.float32
    )
    send_picks = name_hit.astype(jnp.float32)[:, :, :, None] * slot_hit[:, None, :, :]
    rows_sel = jnp.sum(send_picks, axis=1)
    gate_sel = jnp.einsum("tkes,tk->tes", send_picks, gate_weights, precision=highest)
    grad_f32 = grad_y.astype(jnp.float32)
    x_buf = jnp.einsum(
        "tes,td->esd", rows_sel.astype(jnp.bfloat16), tokens, preferred_element_type=jnp.float32
    ).astype(jnp.bfloat16)
    g_buf = jnp.einsum("tes,td->esd", gate_sel, grad_f32, precision=highest).astype(jnp.bfloat16)
    flag = jnp.sum(gate_sel, axis=0)
    flag_cols = (jnp.arange(FLAG_COLS) == 0).astype(jnp.float32)
    flag_buf = (flag[:, :, None] * flag_cols).astype(jnp.bfloat16)
    send = jnp.concatenate([x_buf, g_buf, flag_buf], axis=-1)
    send = send.reshape(local_experts, expert_devs, slot_count, 2 * feature_dim + FLAG_COLS)
    mine = lax.axis_index("expert") * local_experts + jnp.arange(local_experts, dtype=jnp.int32)
    is_hot = jnp.any(mine[:, None] == hot_experts[None, :], axis=1)
    cap_mine = capacity[mine]

    def prepare(recv, hot_e, cap_e, compact):
        valid = (recv[:, 2 * feature_dim] > 0).astype(jnp.int32)
        rank_of = jnp.cumsum(valid) - valid
        keep = (valid > 0) & (hot_e | (rank_of < cap_e))
        rows = jnp.where(keep[:, None], recv[:, : 2 * feature_dim], jnp.zeros((), jnp.bfloat16))
        pick = None
        if compact:
            pick = keep[None, :] & (rank_of[None, :] == jnp.arange(CAP_MAX, dtype=jnp.int32)[:, None])
            pick = pick.astype(jnp.bfloat16)
            rows = jnp.dot(pick, rows, preferred_element_type=jnp.float32).astype(jnp.bfloat16)
        return rows, pick

    def compute(rows_all, weight_in, weight_out):
        rows_all = rows_all[:, None]
        partial_terms, grad_wi, grad_wo = expert_math(
            rows_all[..., :feature_dim], rows_all[..., feature_dim:], weight_in[None], weight_out[None]
        )
        return partial_terms.reshape(-1, feature_dim), grad_wi[0], grad_wo[0]

    def reduce(flat):
        return lax.psum_scatter(flat, "dp", scatter_dimension=0, tiled=True)

    def finish(summed, pick):
        summed = summed.reshape(2, -1, feature_dim)
        if pick is not None:
            summed = jnp.einsum(
                "kr,ckd->crd", pick, summed, preferred_element_type=jnp.float32
            ).astype(jnp.bfloat16)
        summed = summed.reshape(2, expert_devs, slot_count, feature_dim)
        return lax.all_to_all(summed, "expert", split_axis=1, concat_axis=1, tiled=True)

    if split_hot:
        own_a = jnp.argmax(is_hot).astype(jnp.int32)
        owns = [own_a, 1 - own_a]
    else:
        owns = list(range(local_experts))

    def run(compact_last, send, w_in, w_out):
        recvs = []
        for chunk in range(len(owns)):
            chunk_send = send[chunk]
            if recvs:
                chunk_send, recvs[-1] = lax.optimization_barrier((chunk_send, recvs[-1]))
            recvs.append(lax.all_to_all(chunk_send, "expert", split_axis=0, concat_axis=1, tiled=True)[0])
        gathered, picks = [], []
        for chunk, own in enumerate(owns):
            compact = compact_last and chunk == len(owns) - 1
            rows, pick = prepare(recvs[chunk], is_hot[own], cap_mine[own], compact)
            if gathered:
                rows, gathered[-1] = lax.optimization_barrier((rows, gathered[-1]))
            gathered.append(lax.all_gather(rows, "dp", axis=0, tiled=False))
            picks.append(pick)
        flats, grads_wi, grads_wo = [], [], []
        for chunk, own in enumerate(owns):
            rows_all = gathered[chunk]
            if flats:
                rows_all, flats[-1] = lax.optimization_barrier((rows_all, flats[-1]))
            flat, grad_wi, grad_wo = compute(rows_all, w_in[own], w_out[own])
            flats.append(flat)
            grads_wi.append(grad_wi)
            grads_wo.append(grad_wo)
        sums = []
        for flat in flats:
            if sums:
                flat, sums[-1] = lax.optimization_barrier((flat, sums[-1]))
            sums.append(reduce(flat))
        backs = [finish(summed, pick) for summed, pick in zip(sums, picks)]
        back = tuple(backs)
        if split_hot:
            first = owns[0] == 0
            grad_wi = jnp.stack([jnp.where(first, grads_wi[0], grads_wi[1]), jnp.where(first, grads_wi[1], grads_wi[0])])
            grad_wo = jnp.stack([jnp.where(first, grads_wo[0], grads_wo[1]), jnp.where(first, grads_wo[1], grads_wo[0])])
        else:
            grad_wi, grad_wo = jnp.stack(grads_wi), jnp.stack(grads_wo)
        return back, grad_wi, grad_wo

    if split_hot:
        one_hot_each = jnp.all(hot_per_dev <= 1)
        back, grad_wi, grad_wo = lax.cond(
            one_hot_each, partial(run, True), partial(run, False), send, w_in, w_out
        )
    else:
        back, grad_wi, grad_wo = run(False, send, w_in, w_out)
    chunks = len(back)
    gate_c = gate_sel.reshape(tok_rows, chunks, expert_devs, slot_count)
    rows_c = rows_sel.reshape(tok_rows, chunks, expert_devs, slot_count)
    picks_c = send_picks.reshape(tok_rows, top_k, chunks, expert_devs, slot_count)
    mixed, token_grad, gate_grad = 0.0, 0.0, 0.0
    for chunk in range(chunks):
        out_f32 = back[chunk][0].astype(jnp.float32)
        mixed = mixed + jnp.einsum("tes,esd->td", gate_c[:, chunk], out_f32, precision=highest)
        token_grad = token_grad + jnp.einsum(
            "tes,esd->td", rows_c[:, chunk].astype(jnp.bfloat16), back[chunk][1], preferred_element_type=jnp.float32
        )
        dot_vals = jnp.einsum("td,esd->tes", grad_y, back[chunk][0], preferred_element_type=jnp.float32)
        gate_grad = gate_grad + jnp.einsum("tkes,tes->tk", picks_c[:, :, chunk], dot_vals, precision=highest)
    return (
        mixed.astype(jnp.bfloat16),
        token_grad.astype(jnp.bfloat16),
        gate_grad,
        grad_wi.astype(jnp.bfloat16),
        grad_wo.astype(jnp.bfloat16),
    )


def solution(mesh):
    in_specs = (
        P(("dp", "expert"), None),
        P(("dp", "expert"), None),
        P(("dp", "expert"), None),
        P(),
        P(),
        P("expert", None, "dp"),
        P("expert", "dp", None),
        P(("dp", "expert"), None),
    )
    out_specs = (
        P(("dp", "expert"), None),
        P(("dp", "expert"), None),
        P(("dp", "expert"), None),
        P("expert", None, "dp"),
        P("expert", "dp", None),
    )
    return jax.shard_map(local, mesh=mesh, in_specs=in_specs, out_specs=out_specs, check_vma=False)
```
